256 devices in a mesh: dp: 32 (over z, y), expert: 8 (over x, core).
Axes of the slice: x: 4, y: 4, z: 8, core: 2. Of those that a mesh axis runs over, the one named last changes fastest.
Arguments:
- tokens: bfloat16 [32768, 2048], P(('dp', 'expert')), may hold values from -6 to 6
- routes: int32 [32768, 2], P(('dp', 'expert')), may hold values from 0 to 127, all different within a row; in each aligned block of 128 rows (0 to 127, 128 to 255, ...) at most 4 rows name the same one
- gate_codes: int32 [32768, 2], P(('dp', 'expert')), may hold values from 1 to 1024
- w_gate: bfloat16 [256, 2048, 384], P(('dp', 'expert')), may hold values from -0.125 to 0.125
- w_up: bfloat16 [256, 2048, 384], P(('dp', 'expert')), may hold values from -0.125 to 0.125
- w_down: bfloat16 [256, 384, 2048], P(('dp', 'expert')), may hold values from -0.21875 to 0.21875
- cot: bfloat16 [32768, 2048], P(('dp', 'expert')), may hold values from -6 to 6
Outputs:
- mixed: bfloat16 [32768, 2048], P(('dp', 'expert'))
- d_tokens: bfloat16 [32768, 2048], P(('dp', 'expert'))
- d_gate: bfloat16 [256, 2048, 384], P(('dp', 'expert'))
- d_up: bfloat16 [256, 2048, 384], P(('dp', 'expert'))
- d_down: bfloat16 [256, 384, 2048], P(('dp', 'expert'))
The draws below stay inside these ranges and needn't reach their ends.
Inputs may be any that keep to these rules, and one draw needn't show every extreme that they name: `routes`: each row names 2 different experts; among the 128 rows of one device no expert is named more than 4 times, a bound that some block reaches. `gate_codes`: the gate weight is the value divided by 1024.
All inputs are finite; a program needn't handle non-finite values.
Results may differ from the reference program's by a relative error of at most 0.012.
Values may be sent and summed in bfloat16 or wider, within the bound.
No kernel may reach another device: no remote copies, remote signals or barrier semaphores. Data moves between devices by JAX's collectives and lax.ppermute only.
A program may use at most 128 MiB of HBM per device.

```python
import math
import jax
import jax.numpy as jnp
import numpy as np
from jax import lax

D = 2048
F = 768
TOP = 2
TOK_DEV = 128
FH = 384
EXPERTS = 128
SUBS = 256
MOST = 4
TOKENS = 32768
N_DP = 32
N_EXPERT = 8


def plant(values, stream_key, low, high):
    shape = values.shape
    spot = [jax.random.randint(jax.random.fold_in(stream_key, axis), (), 0, shape[axis]) for axis in range(len(shape))]
    values = values.at[tuple(spot)].set(low)
    longest = shape.index(max(shape))
    spot[longest] = (spot[longest] + 1) % shape[longest]
    return values.at[tuple(spot)].set(high)


def levels(stream_key, extent, shards, low, high):
    factor_of, own = 1.0, jax.random.fold_in(stream_key, 6)
    for dim, parts in shards:
        steps = jnp.exp(jax.random.uniform(jax.random.fold_in(own, dim), (parts,), jnp.float32, low / len(shards), high / len(shards)))
        factor_of = factor_of * jnp.repeat(steps, extent[dim] // parts).reshape([-1 if axis == dim else 1 for axis in range(len(extent))])
    return factor_of


def assign_block(key, own, number, rows, amount, top, reach, slope):
    order = jax.random.permutation(key, amount)
    packed, ordinary = portions_of(amount, rows * top, reach, slope, True), portions_of(amount, rows * top, reach, slope, False)
    places = jnp.arange(amount)

    def named(sizes, turn):
        used = int((sizes > 0).sum())
        fixed = max(1, used // 4)
        moved = fixed + (places - fixed + turn * (used - fixed)) % max(1, amount - fixed)
        return jnp.zeros((amount,), jnp.int32).at[order[jnp.where(places < fixed, places, moved)]].set(jnp.asarray(sizes, jnp.int32))

    sizes = jnp.where(number % 4 == 0, named(packed, number // 4), named(ordinary, number - number // 4 - 1))
    mixed = jax.random.permutation(jax.random.fold_in(own, 3), amount)
    donor, receiver = mixed[0:amount // 2 * 2:2], mixed[1:amount // 2 * 2:2]
    slack = jnp.minimum(sizes[donor] - 1, reach - sizes[receiver]) // 2
    slack = jnp.where((donor == order[0]) | (receiver == order[0]) | (sizes[receiver] == 0), 0, jnp.maximum(slack, 0))
    moved = jax.random.randint(jax.random.fold_in(own, 4), (amount // 2,), 0, 1 << 20) % (slack + 1)
    sizes = sizes.at[donor].add(-moved).at[receiver].add(moved)
    items = jnp.searchsorted(jnp.cumsum(sizes), jnp.arange(rows * top), side="right").astype(jnp.int32)
    table = items.reshape(top, rows).T
    table = table[jax.random.permutation(jax.random.fold_in(own, 1), rows)]
    turn = jax.random.randint(jax.random.fold_in(own, 2), (rows, 1), 0, top)
    return jnp.take_along_axis(table, (jnp.arange(top)[None, :] + turn) % top, axis=1)


def portions_of(count, total, reach, slope, full):
    loads = [(1 << 20) // math.isqrt(rank ** slope) + 1 for rank in range(1, count + 1)]
    largest = reach if full else min(reach, max(-(-total // count), total * loads[0] // sum(loads)))
    least = 1 if total - largest >= count - 1 else 0
    holding, spare = [largest] + [least] * (count - 1), total - largest - least * (count - 1)
    while spare > 0:
        candidates = [i for i in range(1, count) if holding[i] < largest] or [i for i in range(1, count) if holding[i] < reach]
        whole, budget = sum([loads[i] for i in candidates]), spare
        for i in candidates:
            more = min(reach - holding[i], max(1, budget * loads[i] // whole), spare)
            holding[i] = holding[i] + more
            spare = spare - more
    return np.array(holding)


def normal_values(own_key, shape, spread, reach, split=(), kind=jnp.bfloat16):
    values = spread * jax.random.normal(own_key, shape, jnp.float32)
    if split:
        values = values * levels(own_key, shape, split, -0.22, 0.18)
    return jnp.clip(values, -reach, reach).astype(kind)


def setup_inputs(seed: int = 0) -> dict:
    key_of = jax.random.split(jax.random.key(seed), 8)
    tokens = normal_values(key_of[0], (TOKENS, D), 1.0, 6.0, ((0, 256),))
    routes_keys = jax.random.split(jax.random.fold_in(key_of[1], 1), TOKENS // TOK_DEV)
    routes_turns = jax.random.permutation(jax.random.fold_in(key_of[1], 3), TOKENS // TOK_DEV)
    routes = jax.vmap(lambda own, number: assign_block(jax.random.fold_in(key_of[1], 2), own, number, TOK_DEV, EXPERTS, TOP, MOST, 2))(routes_keys, routes_turns).reshape((TOKENS, TOP))
    gate_codes = plant(jax.random.randint(key_of[2], (TOKENS, TOP), 1, 1025), jax.random.fold_in(key_of[2], 1), 1, 1024).astype(jnp.int32)
    w_gate = normal_values(key_of[3], (SUBS, D, FH), D ** -0.5, 0.125, ((0, 256),))
    w_up = normal_values(key_of[4], (SUBS, D, FH), D ** -0.5, 0.125, ((0, 256),))
    w_down = normal_values(key_of[5], (SUBS, FH, D), F ** -0.5, 0.21875, ((0, 256),))
    cot = normal_values(key_of[6], (TOKENS, D), 1.0, 6.0, ((0, 256),))
    return dict(tokens=tokens, routes=routes, gate_codes=gate_codes, w_gate=w_gate, w_up=w_up, w_down=w_down, cot=cot)


def rounded(value):
    return lax.optimization_barrier(value.astype(jnp.bfloat16)).astype(jnp.float32)


def reference(tokens, routes, gate_codes, w_gate, w_up, w_down, cot):
    tok_all, top = routes.shape
    width = tokens.shape[1]
    half = w_gate.shape[2]
    experts = w_gate.shape[0] // 2
    capacity = MOST * N_DP * N_EXPERT
    pairs = tok_all * top
    expert_ids = routes.reshape(pairs)
    onehot = (expert_ids[:, None] == jnp.arange(experts, dtype=jnp.int32)[None, :]).astype(jnp.int32)
    before = jnp.cumsum(onehot, axis=0) - onehot
    position = jnp.sum(before * onehot, axis=1).astype(jnp.int32)
    table = jnp.full((experts, capacity), pairs, jnp.int32).at[expert_ids, position].set(jnp.arange(pairs, dtype=jnp.int32))
    gates = gate_codes.reshape(pairs).astype(jnp.float32) / 1024.0
    gates_pad = jnp.concatenate([gates, jnp.zeros((1,), jnp.float32)])
    tok_pad = jnp.concatenate([tokens, jnp.zeros((1, width), jnp.bfloat16)], axis=0)
    cot_pad = jnp.concatenate([cot, jnp.zeros((1, width), jnp.bfloat16)], axis=0)
    wg_full = w_gate.reshape(experts, 2, width, half).transpose(0, 2, 1, 3).reshape(experts, width, 2 * half)
    wu_full = w_up.reshape(experts, 2, width, half).transpose(0, 2, 1, 3).reshape(experts, width, 2 * half)
    wd_full = w_down.reshape(experts, 2 * half, width)

    def one_expert(carry, inputs):
        out_acc, grad_acc = carry
        slots, wg, wu, wd = inputs
        token_idx = jnp.where(slots < pairs, slots // top, tok_all).astype(jnp.int32)
        weight = gates_pad[slots]
        xrows = tok_pad[token_idx]
        act = jnp.dot(xrows, wg, preferred_element_type=jnp.float32)
        upv = jnp.dot(xrows, wu, preferred_element_type=jnp.float32)
        sig = jax.nn.sigmoid(act)
        silu = act * sig
        hidden = (silu * upv).astype(jnp.bfloat16)
        out_lo = rounded(jnp.dot(hidden[:, :half], wd[:half], preferred_element_type=jnp.float32))
        out_hi = rounded(jnp.dot(hidden[:, half:], wd[half:], preferred_element_type=jnp.float32))
        qrows = (weight[:, None] * cot_pad[token_idx].astype(jnp.float32)).astype(jnp.bfloat16)
        dhid = jnp.dot(qrows, wd.T, preferred_element_type=jnp.float32)
        dact = (dhid * upv * sig * (1.0 + act * (1.0 - sig))).astype(jnp.bfloat16)
        dupv = (dhid * silu).astype(jnp.bfloat16)
        grad_lo = rounded(jnp.dot(dact[:, :half], wg[:, :half].T, preferred_element_type=jnp.float32) + jnp.dot(dupv[:, :half], wu[:, :half].T, preferred_element_type=jnp.float32))
        grad_hi = rounded(jnp.dot(dact[:, half:], wg[:, half:].T, preferred_element_type=jnp.float32) + jnp.dot(dupv[:, half:], wu[:, half:].T, preferred_element_type=jnp.float32))
        grad_g = jnp.dot(xrows.T, dact, preferred_element_type=jnp.float32).astype(jnp.bfloat16)
        grad_u = jnp.dot(xrows.T, dupv, preferred_element_type=jnp.float32).astype(jnp.bfloat16)
        grad_d = jnp.dot(hidden.T, qrows, preferred_element_type=jnp.float32).astype(jnp.bfloat16)
        out_acc = out_acc.at[token_idx].add(weight[:, None] * (out_lo + out_hi))
        grad_acc = grad_acc.at[token_idx].add(grad_lo + grad_hi)
        return (out_acc, grad_acc), (grad_g, grad_u, grad_d)

    start = (jnp.zeros((tok_all + 1, width), jnp.float32), jnp.zeros((tok_all + 1, width), jnp.float32))
    (out_acc, grad_acc), (grad_g, grad_u, grad_d) = lax.scan(one_expert, start, (table, wg_full, wu_full, wd_full))
    mixed = out_acc[:tok_all].astype(jnp.bfloat16)
    d_tokens = grad_acc[:tok_all].astype(jnp.bfloat16)
    d_gate = grad_g.reshape(experts, width, 2, half).transpose(0, 2, 1, 3).reshape(2 * experts, width, half)
    d_up = grad_u.reshape(experts, width, 2, half).transpose(0, 2, 1, 3).reshape(2 * experts, width, half)
    d_down = grad_d.reshape(2 * experts, half, width)
    return (mixed, d_tokens, d_gate, d_up, d_down)
```

```python
import jax
import jax.numpy as jnp
from jax import lax
from jax.sharding import Mesh
from jax.sharding import PartitionSpec as P

CHIPS = ("dp", "x")


def expert_work(xrows, qrows, wg, wu, wd):
    act = jnp.dot(xrows, wg, preferred_element_type=jnp.float32)
    upv = jnp.dot(xrows, wu, preferred_element_type=jnp.float32)
    sig = jax.nn.sigmoid(act)
    silu = act * sig
    hidden = (silu * upv).astype(jnp.bfloat16)
    outv = jnp.dot(hidden, wd, preferred_element_type=jnp.float32).astype(jnp.bfloat16)
    dhid = jnp.dot(qrows, wd.T, preferred_element_type=jnp.float32)
    dact = (dhid * upv * sig * (1.0 + act * (1.0 - sig))).astype(jnp.bfloat16)
    dupv = (dhid * silu).astype(jnp.bfloat16)
    pgrad = (
        jnp.dot(dact, wg.T, preferred_element_type=jnp.float32)
        + jnp.dot(dupv, wu.T, preferred_element_type=jnp.float32)
    ).astype(jnp.bfloat16)
    grad_g = jnp.dot(xrows.T, dact, preferred_element_type=jnp.float32)
    grad_u = jnp.dot(xrows.T, dupv, preferred_element_type=jnp.float32)
    grad_d = jnp.dot(hidden.T, qrows, preferred_element_type=jnp.float32)
    return outv, pgrad, grad_g, grad_u, grad_d


def local(tokens, routes, gate_codes, w_gate, w_up, w_down, cot):
    tok_rows, top = routes.shape
    width = tokens.shape[1]
    half = w_gate.shape[2]
    chips = lax.axis_size("dp") * lax.axis_size("x")
    pairs = tok_rows * top
    most = max(1, 2 * pairs // chips)
    slots = chips * most
    core = lax.axis_index("core")
    swap = [(0, 1), (1, 0)]

    wg_o, wu_o, wd_o = lax.ppermute((w_gate[0], w_up[0], w_down[0]), "core", swap)
    first = core == 0
    wg = jnp.where(first, jnp.concatenate([w_gate[0], wg_o], 1), jnp.concatenate([wg_o, w_gate[0]], 1))
    wu = jnp.where(first, jnp.concatenate([w_up[0], wu_o], 1), jnp.concatenate([wu_o, w_up[0]], 1))
    wd = jnp.where(first, jnp.concatenate([w_down[0], wd_o], 0), jnp.concatenate([wd_o, w_down[0]], 0))

    expert_ids = routes.reshape(pairs)
    onehot = (expert_ids[:, None] == jnp.arange(chips, dtype=jnp.int32)[None, :]).astype(jnp.int32)
    before = jnp.cumsum(onehot, axis=0) - onehot
    position = jnp.sum(before * onehot, axis=1)
    slot = expert_ids * most + position
    gates = gate_codes.reshape(pairs).astype(jnp.float32) / 1024.0
    qpairs = (
        (gates.reshape(tok_rows, top, 1) * cot.astype(jnp.float32)[:, None, :])
        .astype(jnp.bfloat16)
        .reshape(pairs, width)
    )
    pick = (slot.reshape(tok_rows, top).T[:, :, None] == jnp.arange(slots, dtype=jnp.int32)[None, None, :])
    pick = pick.astype(jnp.bfloat16)
    sel_x = pick[0] + pick[1]
    xs = jnp.dot(sel_x.T, tokens, preferred_element_type=jnp.float32).astype(jnp.bfloat16)
    sel_q = pick.transpose(2, 1, 0).reshape(slots, pairs)
    qs = jnp.dot(sel_q, qpairs, preferred_element_type=jnp.float32).astype(jnp.bfloat16)
    send = jnp.concatenate([xs, qs], axis=1).reshape(chips, most, 2 * width)
    recv = lax.all_to_all(send, CHIPS, 0, 0, tiled=True).reshape(slots, 2 * width)

    outv, pgrad, grad_g, grad_u, grad_d = expert_work(recv[:, :width], recv[:, width:], wg, wu, wd)

    back = jnp.concatenate([outv, pgrad], axis=1).reshape(chips, most, 2 * width)
    got = lax.all_to_all(back, CHIPS, 0, 0, tiled=True).reshape(slots, 2 * width)

    g_lo, g_hi = grad_g[:, :half], grad_g[:, half:]
    u_lo, u_hi = grad_u[:, :half], grad_u[:, half:]
    d_lo, d_hi = grad_d[:half], grad_d[half:]
    mine = (jnp.where(first, g_lo, g_hi), jnp.where(first, u_lo, u_hi), jnp.where(first, d_lo, d_hi))
    other = (jnp.where(first, g_hi, g_lo), jnp.where(first, u_hi, u_lo), jnp.where(first, d_hi, d_lo))
    came = lax.ppermute(other, "core", swap)
    d_gate = (mine[0] + came[0]).astype(jnp.bfloat16)
    d_up = (mine[1] + came[1]).astype(jnp.bfloat16)
    d_down = (mine[2] + came[2]).astype(jnp.bfloat16)

    o_k = jnp.einsum("kts,sw->ktw", pick, got[:, :width], preferred_element_type=jnp.float32)
    mixed = (gates.reshape(tok_rows, top).T[:, :, None] * o_k).sum(0).astype(jnp.bfloat16)
    d_tokens = jnp.dot(sel_x, got[:, width:], preferred_element_type=jnp.float32).astype(jnp.bfloat16)
    return (mixed, d_tokens, d_gate[None], d_up[None], d_down[None])


def solution(mesh):
    n_data = mesh.shape["dp"]
    n_group = mesh.shape["expert"]
    fine = Mesh(mesh.devices.reshape(n_data, n_group // 2, 2), ("dp", "x", "core"))
    rows = P(("dp", "x", "core"), None)
    stack = P(("dp", "x", "core"), None, None)
    return jax.shard_map(
        local,
        mesh=fine,
        in_specs=(rows, rows, rows, stack, stack, stack, rows),
        out_specs=(rows, rows, stack, stack, stack),
        check_vma=False,
    )
```

```python
import jax
import jax.numpy as jnp
from jax import lax
from jax.sharding import Mesh
from jax.sharding import PartitionSpec as P

CHIPS = ("dp", "x")


def local(tokens, routes, gate_codes, w_gate, w_up, w_down, cot):
    tok_rows, top = routes.shape
    width = tokens.shape[1]
    half = w_gate.shape[2]
    chips = lax.axis_size("dp") * lax.axis_size("x")
    pairs = tok_rows * top
    most = max(1, 2 * pairs // chips)
    slots = chips * most
    core = lax.axis_index("core")
    swap = [(0, 1), (1, 0)]
    f32 = jnp.float32

    wg_o, wu_o, wd_o = lax.ppermute((w_gate[0], w_up[0], w_down[0]), "core", swap)
    first = core == 0
    wg = jnp.where(first, jnp.concatenate([w_gate[0], wg_o], 1), jnp.concatenate([wg_o, w_gate[0]], 1))
    wu = jnp.where(first, jnp.concatenate([w_up[0], wu_o], 1), jnp.concatenate([wu_o, w_up[0]], 1))
    wd = jnp.where(first, jnp.concatenate([w_down[0], wd_o], 0), jnp.concatenate([wd_o, w_down[0]], 0))

    expert_ids = routes.reshape(pairs)
    onehot = (expert_ids[:, None] == jnp.arange(chips, dtype=jnp.int32)[None, :]).astype(jnp.int32)
    before = jnp.cumsum(onehot, axis=0) - onehot
    position = jnp.sum(before * onehot, axis=1)
    slot = expert_ids * most + position
    gates = gate_codes.reshape(pairs).astype(f32) / 1024.0
    qpairs = (
        (gates.reshape(tok_rows, top, 1) * cot.astype(f32)[:, None, :])
        .astype(jnp.bfloat16)
        .reshape(pairs, width)
    )
    pick = slot.reshape(tok_rows, top).T[:, :, None] == jnp.arange(slots, dtype=jnp.int32)[None, None, :]
    pick = pick.astype(jnp.bfloat16)
    sel_x = (pick[0] + pick[1]).reshape(tok_rows, chips, most)
    sel_q = pick.transpose(2, 1, 0).reshape(chips, most, pairs)

    xs = jnp.einsum("tds,tw->dsw", sel_x, tokens, preferred_element_type=f32).astype(jnp.bfloat16)
    xrows = lax.all_to_all(xs, CHIPS, 0, 0, tiled=True)
    qs = jnp.einsum("dsp,pw->dsw", sel_q, qpairs, preferred_element_type=f32).astype(jnp.bfloat16)
    qrows = lax.all_to_all(qs, CHIPS, 0, 0, tiled=True)

    act = jnp.einsum("dsw,wf->dsf", xrows, wg, preferred_element_type=f32)
    upv = jnp.einsum("dsw,wf->dsf", xrows, wu, preferred_element_type=f32)
    sig = jax.nn.sigmoid(act)
    silu = act * sig
    hidden = (silu * upv).astype(jnp.bfloat16)
    outv = jnp.einsum("dsf,fw->dsw", hidden, wd, preferred_element_type=f32).astype(jnp.bfloat16)
    qrows, outv = lax.optimization_barrier((qrows, outv))
    o_back = lax.all_to_all(outv, CHIPS, 0, 0, tiled=True)

    dhid = jnp.einsum("dsw,fw->dsf", qrows, wd, preferred_element_type=f32)
    dact = (dhid * upv * sig * (1.0 + act * (1.0 - sig))).astype(jnp.bfloat16)
    dupv = (dhid * silu).astype(jnp.bfloat16)
    pgrad = (
        jnp.einsum("dsf,wf->dsw", dact, wg, preferred_element_type=f32)
        + jnp.einsum("dsf,wf->dsw", dupv, wu, preferred_element_type=f32)
    ).astype(jnp.bfloat16)
    pgrad, o_back = lax.optimization_barrier((pgrad, o_back))
    p_back = lax.all_to_all(pgrad, CHIPS, 0, 0, tiled=True)

    grad_g = jnp.einsum("dsw,dsf->wf", xrows, dact, preferred_element_type=f32)
    grad_u = jnp.einsum("dsw,dsf->wf", xrows, dupv, preferred_element_type=f32)
    grad_d = jnp.einsum("dsf,dsw->fw", hidden, qrows, preferred_element_type=f32)
    g_lo, g_hi = grad_g[:, :half], grad_g[:, half:]
    u_lo, u_hi = grad_u[:, :half], grad_u[:, half:]
    d_lo, d_hi = grad_d[:half], grad_d[half:]
    mine = (jnp.where(first, g_lo, g_hi), jnp.where(first, u_lo, u_hi), jnp.where(first, d_lo, d_hi))
    other = (jnp.where(first, g_hi, g_lo), jnp.where(first, u_hi, u_lo), jnp.where(first, d_hi, d_lo))
    came = lax.ppermute(other, "core", swap)
    d_gate = (mine[0] + came[0]).astype(jnp.bfloat16)
    d_up = (mine[1] + came[1]).astype(jnp.bfloat16)
    d_down = (mine[2] + came[2]).astype(jnp.bfloat16)

    pick4 = pick.reshape(top, tok_rows, chips, most)
    o_k = jnp.einsum("ktds,dsw->ktw", pick4, o_back, preferred_element_type=f32)
    mixed = (gates.reshape(tok_rows, top).T[:, :, None] * o_k).sum(0).astype(jnp.bfloat16)
    d_tokens = jnp.einsum("tds,dsw->tw", sel_x, p_back, preferred_element_type=f32).astype(jnp.bfloat16)
    return (mixed, d_tokens, d_gate[None], d_up[None], d_down[None])


def solution(mesh):
    n_data = mesh.shape["dp"]
    n_group = mesh.shape["expert"]
    fine = Mesh(mesh.devices.reshape(n_data, n_group // 2, 2), ("dp", "x", "core"))
    rows = P(("dp", "x", "core"), None)
    stack = P(("dp", "x", "core"), None, None)
    return jax.shard_map(
        local,
        mesh=fine,
        in_specs=(rows, rows, rows, stack, stack, stack, rows),
        out_specs=(rows, rows, stack, stack, stack),
        check_vma=False,
    )
```

```python
import jax
import jax.numpy as jnp
from jax import lax
from jax.sharding import Mesh
from jax.sharding import PartitionSpec as P

CHIPS = ("dp", "x")


def pack(rows, chips):
    return rows.reshape(chips, -1, rows.shape[1])


def to_chips(packed):
    sent = lax.all_to_all(packed, CHIPS, 0, 0, tiled=True)
    return sent.reshape(-1, packed.shape[2])


def local(tokens, routes, gate_codes, w_gate, w_up, w_down, cot):
    tok_rows, top = routes.shape
    width = tokens.shape[1]
    half = w_gate.shape[2]
    chips = lax.axis_size("dp") * lax.axis_size("x")
    pairs = tok_rows * top
    most = max(1, 2 * pairs // chips)
    slots = chips * most
    core = lax.axis_index("core")
    swap = [(0, 1), (1, 0)]
    f32 = jnp.float32

    wg_o, wu_o, wd_o = lax.ppermute((w_gate[0], w_up[0], w_down[0]), "core", swap)
    first = core == 0
    wg = jnp.where(first, jnp.concatenate([w_gate[0], wg_o], 1), jnp.concatenate([wg_o, w_gate[0]], 1))
    wu = jnp.where(first, jnp.concatenate([w_up[0], wu_o], 1), jnp.concatenate([wu_o, w_up[0]], 1))
    wd = jnp.where(first, jnp.concatenate([w_down[0], wd_o], 0), jnp.concatenate([wd_o, w_down[0]], 0))

    expert_ids = routes.reshape(pairs)
    onehot = (expert_ids[:, None] == jnp.arange(chips, dtype=jnp.int32)[None, :]).astype(jnp.int32)
    before = jnp.cumsum(onehot, axis=0) - onehot
    position = jnp.sum(before * onehot, axis=1)
    slot = expert_ids * most + position
    gates = gate_codes.reshape(pairs).astype(f32) / 1024.0
    qpairs = (
        (gates.reshape(tok_rows, top, 1) * cot.astype(f32)[:, None, :])
        .astype(jnp.bfloat16)
        .reshape(pairs, width)
    )
    pick = slot.reshape(tok_rows, top).T[:, :, None] == jnp.arange(slots, dtype=jnp.int32)[None, None, :]
    pick = pick.astype(jnp.bfloat16)
    sel_x = (pick[0] + pick[1]).reshape(tok_rows, chips, most)
    sel_q = pick.transpose(2, 1, 0).reshape(chips, most, pairs)

    sel_x2 = sel_x.reshape(tok_rows, slots)
    xs = jnp.dot(sel_x2.T, tokens, preferred_element_type=f32).astype(jnp.bfloat16)
    xrows = to_chips(pack(xs, chips))
    qs = jnp.dot(sel_q.reshape(slots, pairs), qpairs, preferred_element_type=f32).astype(jnp.bfloat16)
    qs, xrows = lax.optimization_barrier((pack(qs, chips), xrows))
    qrows = to_chips(qs)

    act = jnp.dot(xrows, wg, preferred_element_type=f32)
    upv = jnp.dot(xrows, wu, preferred_element_type=f32)
    sig = jax.nn.sigmoid(act)
    silu = act * sig
    hidden = (silu * upv).astype(jnp.bfloat16)
    outv = jnp.dot(hidden, wd, preferred_element_type=f32).astype(jnp.bfloat16)
    qrows, outv = lax.optimization_barrier((qrows, pack(outv, chips)))
    o_back = to_chips(outv)

    dhid = jnp.dot(qrows, wd.T, preferred_element_type=f32)
    dact = (dhid * upv * sig * (1.0 + act * (1.0 - sig))).astype(jnp.bfloat16)
    dupv = (dhid * silu).astype(jnp.bfloat16)
    pgrad = (
        jnp.dot(dact, wg.T, preferred_element_type=f32)
        + jnp.dot(dupv, wu.T, preferred_element_type=f32)
    ).astype(jnp.bfloat16)
    pgrad, o_back = lax.optimization_barrier((pack(pgrad, chips), o_back))
    p_back = to_chips(pgrad)

    grad_g = jnp.dot(xrows.T, dact, preferred_element_type=f32)
    grad_u = jnp.dot(xrows.T, dupv, preferred_element_type=f32)
    grad_d = jnp.dot(hidden.T, qrows, preferred_element_type=f32)
    g_lo, g_hi = grad_g[:, :half], grad_g[:, half:]
    u_lo, u_hi = grad_u[:, :half], grad_u[:, half:]
    d_lo, d_hi = grad_d[:half], grad_d[half:]
    mine = (jnp.where(first, g_lo, g_hi), jnp.where(first, u_lo, u_hi), jnp.where(first, d_lo, d_hi))
    other = (jnp.where(first, g_hi, g_lo), jnp.where(first, u_hi, u_lo), jnp.where(first, d_hi, d_lo))
    came = lax.ppermute(other, "core", swap)
    d_gate = (mine[0] + came[0]).astype(jnp.bfloat16)
    d_up = (mine[1] + came[1]).astype(jnp.bfloat16)
    d_down = (mine[2] + came[2]).astype(jnp.bfloat16)

    o_k = jnp.einsum("kts,sw->ktw", pick, o_back, preferred_element_type=f32)
    mixed = (gates.reshape(tok_rows, top).T[:, :, None] * o_k).sum(0).astype(jnp.bfloat16)
    d_tokens = jnp.dot(sel_x2, p_back, preferred_element_type=f32).astype(jnp.bfloat16)
    return (mixed, d_tokens, d_gate[None], d_up[None], d_down[None])


def solution(mesh):
    n_data = mesh.shape["dp"]
    n_group = mesh.shape["expert"]
    fine = Mesh(mesh.devices.reshape(n_data, n_group // 2, 2), ("dp", "x", "core"))
    rows = P(("dp", "x", "core"), None)
    stack = P(("dp", "x", "core"), None, None)
    return jax.shard_map(
        local,
        mesh=fine,
        in_specs=(rows, rows, rows, stack, stack, stack, rows),
        out_specs=(rows, rows, stack, stack, stack),
        check_vma=False,
    )
```

```python
import jax
import jax.numpy as jnp
from jax import lax
from jax.sharding import Mesh
from jax.sharding import PartitionSpec as P

CHIPS = ("dp", "x")


def pack(rows, chips):
    return rows.reshape(chips, -1, rows.shape[1])


def to_chips(packed):
    return lax.all_to_all(packed, CHIPS, 0, 0, tiled=True)


def unpack(sent):
    return sent.reshape(-1, sent.shape[2])


def local(tokens, routes, gate_codes, w_gate, w_up, w_down, cot):
    tok_rows, top = routes.shape
    width = tokens.shape[1]
    half = w_gate.shape[2]
    chips = lax.axis_size("dp") * lax.axis_size("x")
    pairs = tok_rows * top
    most = max(1, 2 * pairs // chips)
    slots = chips * most
    core = lax.axis_index("core")
    swap = [(0, 1), (1, 0)]
    f32 = jnp.float32

    wg_o, wu_o, wd_o = lax.ppermute((w_gate[0], w_up[0], w_down[0]), "core", swap)
    first = core == 0
    wg = jnp.where(first, jnp.concatenate([w_gate[0], wg_o], 1), jnp.concatenate([wg_o, w_gate[0]], 1))
    wu = jnp.where(first, jnp.concatenate([w_up[0], wu_o], 1), jnp.concatenate([wu_o, w_up[0]], 1))
    wd = jnp.where(first, jnp.concatenate([w_down[0], wd_o], 0), jnp.concatenate([wd_o, w_down[0]], 0))

    expert_ids = routes.reshape(pairs)
    onehot = (expert_ids[:, None] == jnp.arange(chips, dtype=jnp.int32)[None, :]).astype(jnp.int32)
    before = jnp.cumsum(onehot, axis=0) - onehot
    position = jnp.sum(before * onehot, axis=1)
    slot = expert_ids * most + position
    gates = gate_codes.reshape(pairs).astype(f32) / 1024.0
    qpairs = (
        (gates.reshape(tok_rows, top, 1) * cot.astype(f32)[:, None, :])
        .astype(jnp.bfloat16)
        .reshape(pairs, width)
    )
    pick = slot.reshape(tok_rows, top).T[:, :, None] == jnp.arange(slots, dtype=jnp.int32)[None, None, :]
    pick = pick.astype(jnp.bfloat16)
    sel_x = (pick[0] + pick[1]).reshape(tok_rows, chips, most)
    sel_q = pick.transpose(2, 1, 0).reshape(chips, most, pairs)

    sel_x2 = sel_x.reshape(tok_rows, slots)
    xs = jnp.dot(sel_x2.T, tokens, preferred_element_type=f32).astype(jnp.bfloat16)
    xrows = to_chips(pack(xs, chips))
    qs = jnp.dot(sel_q.reshape(slots, pairs), qpairs, preferred_element_type=f32).astype(jnp.bfloat16)
    qs, xrows = lax.optimization_barrier((pack(qs, chips), xrows))
    xrows = unpack(xrows)
    qrows = to_chips(qs)

    act = jnp.dot(xrows, wg, preferred_element_type=f32)
    upv = jnp.dot(xrows, wu, preferred_element_type=f32)
    sig = jax.nn.sigmoid(act)
    silu = act * sig
    hidden = (silu * upv).astype(jnp.bfloat16)
    outv = jnp.dot(hidden, wd, preferred_element_type=f32).astype(jnp.bfloat16)
    qrows, outv = lax.optimization_barrier((qrows, pack(outv, chips)))
    qrows = unpack(qrows)
    o_back = to_chips(outv)

    dhid = jnp.dot(qrows, wd.T, preferred_element_type=f32)
    dact = (dhid * upv * sig * (1.0 + act * (1.0 - sig))).astype(jnp.bfloat16)
    dupv = (dhid * silu).astype(jnp.bfloat16)
    pgrad = (
        jnp.dot(dact, wg.T, preferred_element_type=f32)
        + jnp.dot(dupv, wu.T, preferred_element_type=f32)
    ).astype(jnp.bfloat16)
    pgrad, o_back = lax.optimization_barrier((pack(pgrad, chips), o_back))
    o_back = unpack(o_back)
    p_back = unpack(to_chips(pgrad))

    grad_g = jnp.dot(xrows.T, dact, preferred_element_type=f32)
    grad_u = jnp.dot(xrows.T, dupv, preferred_element_type=f32)
    grad_d = jnp.dot(hidden.T, qrows, preferred_element_type=f32)
    g_lo, g_hi = grad_g[:, :half], grad_g[:, half:]
    u_lo, u_hi = grad_u[:, :half], grad_u[:, half:]
    d_lo, d_hi = grad_d[:half], grad_d[half:]
    mine = (jnp.where(first, g_lo, g_hi), jnp.where(first, u_lo, u_hi), jnp.where(first, d_lo, d_hi))
    other = (jnp.where(first, g_hi, g_lo), jnp.where(first, u_hi, u_lo), jnp.where(first, d_hi, d_lo))
    came = lax.ppermute(other, "core", swap)
    d_gate = (mine[0] + came[0]).astype(jnp.bfloat16)
    d_up = (mine[1] + came[1]).astype(jnp.bfloat16)
    d_down = (mine[2] + came[2]).astype(jnp.bfloat16)

    o_k = jnp.einsum("kts,sw->ktw", pick, o_back, preferred_element_type=f32)
    mixed = (gates.reshape(tok_rows, top).T[:, :, None] * o_k).sum(0).astype(jnp.bfloat16)
    d_tokens = jnp.dot(sel_x2, p_back, preferred_element_type=f32).astype(jnp.bfloat16)
    return (mixed, d_tokens, d_gate[None], d_up[None], d_down[None])


def solution(mesh):
    n_data = mesh.shape["dp"]
    n_group = mesh.shape["expert"]
    fine = Mesh(mesh.devices.reshape(n_data, n_group // 2, 2), ("dp", "x", "core"))
    rows = P(("dp", "x", "core"), None)
    stack = P(("dp", "x", "core"), None, None)
    return jax.shard_map(
        local,
        mesh=fine,
        in_specs=(rows, rows, rows, stack, stack, stack, rows),
        out_specs=(rows, rows, stack, stack, stack),
        check_vma=False,
    )
```

```python
import jax
import jax.numpy as jnp
from jax import lax
from jax.sharding import Mesh
from jax.sharding import PartitionSpec as P

CHIPS = ("dp", "x")


def pack(rows, chips):
    return rows.reshape(chips, -1, rows.shape[1])


def to_chips(packed):
    return lax.all_to_all(packed, CHIPS, 0, 0, tiled=True)


def unpack(sent):
    return sent.reshape(-1, sent.shape[2])


def local(tokens, routes, gate_codes, w_gate, w_up, w_down, cot):
    tok_rows, top = routes.shape
    width = tokens.shape[1]
    half = w_gate.shape[2]
    chips = lax.axis_size("dp") * lax.axis_size("x")
    pairs = tok_rows * top
    most = max(1, 2 * pairs // chips)
    slots = chips * most
    core = lax.axis_index("core")
    swap = [(0, 1), (1, 0)]
    f32 = jnp.float32

    wg_o, wu_o, wd_o = lax.ppermute((w_gate[0], w_up[0], w_down[0]), "core", swap)
    first = core == 0
    wg = jnp.where(first, jnp.concatenate([w_gate[0], wg_o], 1), jnp.concatenate([wg_o, w_gate[0]], 1))
    wu = jnp.where(first, jnp.concatenate([w_up[0], wu_o], 1), jnp.concatenate([wu_o, w_up[0]], 1))
    wd = jnp.where(first, jnp.concatenate([w_down[0], wd_o], 0), jnp.concatenate([wd_o, w_down[0]], 0))

    expert_ids = routes.reshape(pairs)
    onehot = (expert_ids[:, None] == jnp.arange(chips, dtype=jnp.int32)[None, :]).astype(jnp.int32)
    before = jnp.cumsum(onehot, axis=0) - onehot
    position = jnp.sum(before * onehot, axis=1)
    slot = expert_ids * most + position
    gates = gate_codes.reshape(pairs).astype(f32) / 1024.0
    qpairs = (
        (gates.reshape(tok_rows, top, 1) * cot.astype(f32)[:, None, :])
        .astype(jnp.bfloat16)
        .reshape(pairs, width)
    )
    pick = slot.reshape(tok_rows, top).T[:, :, None] == jnp.arange(slots, dtype=jnp.int32)[None, None, :]
    pick = pick.astype(jnp.bfloat16)
    sel_x = (pick[0] + pick[1]).reshape(tok_rows, chips, most)
    sel_q = pick.transpose(2, 1, 0).reshape(chips, most, pairs)

    sel_x2 = sel_x.reshape(tok_rows, slots)
    xs = jnp.dot(sel_x2.T, tokens, preferred_element_type=f32).astype(jnp.bfloat16)
    xrows = to_chips(pack(xs, chips))
    qs = jnp.dot(sel_q.reshape(slots, pairs), qpairs, preferred_element_type=f32).astype(jnp.bfloat16)
    qs, xrows = lax.optimization_barrier((pack(qs, chips), xrows))
    xrows = unpack(xrows)
    qrows = to_chips(qs)

    act = jnp.dot(xrows, wg, preferred_element_type=f32)
    upv = jnp.dot(xrows, wu, preferred_element_type=f32)
    sig = jax.nn.sigmoid(act)
    silu = act * sig
    hidden = (silu * upv).astype(jnp.bfloat16)
    outv = jnp.dot(hidden, wd, preferred_element_type=f32).astype(jnp.bfloat16)
    qrows, outv = lax.optimization_barrier((qrows, pack(outv, chips)))
    qrows = unpack(qrows)
    o_back = to_chips(outv)

    dhid = jnp.dot(qrows, wd.T, preferred_element_type=f32)
    dact = (dhid * upv * sig * (1.0 + act * (1.0 - sig))).astype(jnp.bfloat16)
    dupv = (dhid * silu).astype(jnp.bfloat16)
    pgrad = (
        jnp.dot(dact, wg.T, preferred_element_type=f32)
        + jnp.dot(dupv, wu.T, preferred_element_type=f32)
    ).astype(jnp.bfloat16)
    pgrad, o_back, dact, dupv, hidden = lax.optimization_barrier((pack(pgrad, chips), o_back, dact, dupv, hidden))
    o_back = unpack(o_back)
    p_back = unpack(to_chips(pgrad))

    grad_g = jnp.dot(xrows.T, dact, preferred_element_type=f32)
    grad_u = jnp.dot(xrows.T, dupv, preferred_element_type=f32)
    grad_d = jnp.dot(hidden.T, qrows, preferred_element_type=f32)
    g_lo, g_hi = grad_g[:, :half], grad_g[:, half:]
    u_lo, u_hi = grad_u[:, :half], grad_u[:, half:]
    d_lo, d_hi = grad_d[:half], grad_d[half:]
    mine = (jnp.where(first, g_lo, g_hi), jnp.where(first, u_lo, u_hi), jnp.where(first, d_lo, d_hi))
    other = (jnp.where(first, g_hi, g_lo), jnp.where(first, u_hi, u_lo), jnp.where(first, d_hi, d_lo))
    came = lax.ppermute(other, "core", swap)
    d_gate = (mine[0] + came[0]).astype(jnp.bfloat16)
    d_up = (mine[1] + came[1]).astype(jnp.bfloat16)
    d_down = (mine[2] + came[2]).astype(jnp.bfloat16)

    o_k = jnp.einsum("kts,sw->ktw", pick, o_back, preferred_element_type=f32)
    mixed = (gates.reshape(tok_rows, top).T[:, :, None] * o_k).sum(0).astype(jnp.bfloat16)
    d_tokens = jnp.dot(sel_x2, p_back, preferred_element_type=f32).astype(jnp.bfloat16)
    return (mixed, d_tokens, d_gate[None], d_up[None], d_down[None])


def solution(mesh):
    n_data = mesh.shape["dp"]
    n_group = mesh.shape["expert"]
    fine = Mesh(mesh.devices.reshape(n_data, n_group // 2, 2), ("dp", "x", "core"))
    rows = P(("dp", "x", "core"), None)
    stack = P(("dp", "x", "core"), None, None)
    return jax.shard_map(
        local,
        mesh=fine,
        in_specs=(rows, rows, rows, stack, stack, stack, rows),
        out_specs=(rows, rows, stack, stack, stack),
        check_vma=False,
    )
```

```python
import jax
import jax.numpy as jnp
from jax import lax
from jax.sharding import Mesh
from jax.sharding import PartitionSpec as P

CHIPS = ("dp", "x")


def pack(rows, chips):
    return rows.reshape(chips, -1, rows.shape[1])


def to_chips(packed):
    return lax.all_to_all(packed, CHIPS, 0, 0, tiled=True)


def unpack(sent):
    return sent.reshape(-1, sent.shape[2])


def local(tokens, routes, gate_codes, w_gate, w_up, w_down, cot):
    tok_rows, top = routes.shape
    width = tokens.shape[1]
    half = w_gate.shape[2]
    chips = lax.axis_size("dp") * lax.axis_size("x")
    pairs = tok_rows * top
    most = max(1, 2 * pairs // chips)
    slots = chips * most
    core = lax.axis_index("core")
    swap = [(0, 1), (1, 0)]
    f32 = jnp.float32

    wg_o, wu_o, wd_o = lax.ppermute((w_gate[0], w_up[0], w_down[0]), "core", swap)
    first = core == 0
    wg = jnp.where(first, jnp.concatenate([w_gate[0], wg_o], 1), jnp.concatenate([wg_o, w_gate[0]], 1))
    wu = jnp.where(first, jnp.concatenate([w_up[0], wu_o], 1), jnp.concatenate([wu_o, w_up[0]], 1))
    wd = jnp.where(first, jnp.concatenate([w_down[0], wd_o], 0), jnp.concatenate([wd_o, w_down[0]], 0))

    expert_ids = routes.reshape(pairs)
    onehot = (expert_ids[:, None] == jnp.arange(chips, dtype=jnp.int32)[None, :]).astype(jnp.int32)
    before = jnp.cumsum(onehot, axis=0) - onehot
    position = jnp.sum(before * onehot, axis=1)
    slot = expert_ids * most + position
    gates = gate_codes.reshape(pairs).astype(f32) / 1024.0
    qpairs = (
        (gates.reshape(tok_rows, top, 1) * cot.astype(f32)[:, None, :])
        .astype(jnp.bfloat16)
        .reshape(pairs, width)
    )
    pick = slot.reshape(tok_rows, top).T[:, :, None] == jnp.arange(slots, dtype=jnp.int32)[None, None, :]
    pick = pick.astype(jnp.bfloat16)
    sel_x = (pick[0] + pick[1]).reshape(tok_rows, chips, most)
    sel_q = pick.transpose(2, 1, 0).reshape(chips, most, pairs)

    sel_x2 = sel_x.reshape(tok_rows, slots)
    xs = jnp.dot(sel_x2.T, tokens, preferred_element_type=f32).astype(jnp.bfloat16)
    xrows = to_chips(pack(xs, chips))
    qs = jnp.dot(sel_q.reshape(slots, pairs), qpairs, preferred_element_type=f32).astype(jnp.bfloat16)
    qs, xrows = lax.optimization_barrier((pack(qs, chips), xrows))
    xrows = unpack(xrows)
    qrows = to_chips(qs)

    act = jnp.dot(xrows, wg, preferred_element_type=f32)
    upv = jnp.dot(xrows, wu, preferred_element_type=f32)
    sig = jax.nn.sigmoid(act)
    silu = act * sig
    hidden = (silu * upv).astype(jnp.bfloat16)
    outv = jnp.dot(hidden, wd, preferred_element_type=f32).astype(jnp.bfloat16)
    qrows, outv = lax.optimization_barrier((qrows, pack(outv, chips)))
    qrows = unpack(qrows)
    o_back = to_chips(outv)

    dhid = jnp.dot(qrows, wd.T, preferred_element_type=f32)
    dact = (dhid * upv * sig * (1.0 + act * (1.0 - sig))).astype(jnp.bfloat16)
    dupv = (dhid * silu).astype(jnp.bfloat16)
    pgrad = (
        jnp.dot(dact, wg.T, preferred_element_type=f32)
        + jnp.dot(dupv, wu.T, preferred_element_type=f32)
    ).astype(jnp.bfloat16)
    pgrad, o_back, dact, dupv, hidden = lax.optimization_barrier((pack(pgrad, chips), o_back, dact, dupv, hidden))
    o_back = unpack(o_back)
    p_back = unpack(to_chips(pgrad))

    def halves(value):
        lo, hi = value[:, :half], value[:, half:]
        return jnp.where(first, lo, hi), jnp.where(first, hi, lo)

    dact_m, dact_o = halves(dact)
    dupv_m, dupv_o = halves(dupv)
    hid_m, hid_o = halves(hidden)
    other = (
        jnp.dot(xrows.T, dact_o, preferred_element_type=f32),
        jnp.dot(xrows.T, dupv_o, preferred_element_type=f32),
        jnp.dot(hid_o.T, qrows, preferred_element_type=f32),
    )
    came = lax.ppermute(other, "core", swap)
    d_gate = (jnp.dot(xrows.T, dact_m, preferred_element_type=f32) + came[0]).astype(jnp.bfloat16)
    d_up = (jnp.dot(xrows.T, dupv_m, preferred_element_type=f32) + came[1]).astype(jnp.bfloat16)
    d_down = (jnp.dot(hid_m.T, qrows, preferred_element_type=f32) + came[2]).astype(jnp.bfloat16)

    o_k = jnp.einsum("kts,sw->ktw", pick, o_back, preferred_element_type=f32)
    mixed = (gates.reshape(tok_rows, top).T[:, :, None] * o_k).sum(0).astype(jnp.bfloat16)
    d_tokens = jnp.dot(sel_x2, p_back, preferred_element_type=f32).astype(jnp.bfloat16)
    return (mixed, d_tokens, d_gate[None], d_up[None], d_down[None])


def solution(mesh):
    n_data = mesh.shape["dp"]
    n_group = mesh.shape["expert"]
    fine = Mesh(mesh.devices.reshape(n_data, n_group // 2, 2), ("dp", "x", "core"))
    rows = P(("dp", "x", "core"), None)
    stack = P(("dp", "x", "core"), None, None)
    return jax.shard_map(
        local,
        mesh=fine,
        in_specs=(rows, rows, rows, stack, stack, stack, rows),
        out_specs=(rows, rows, stack, stack, stack),
        check_vma=False,
    )
```

```python
import jax
import jax.numpy as jnp
from jax import lax
from jax.sharding import Mesh
from jax.sharding import PartitionSpec as P

CHIPS = ("dp", "x")


def pack(rows, chips):
    return rows.reshape(chips, -1, rows.shape[1])


def to_chips(packed):
    return lax.all_to_all(packed, CHIPS, 0, 0, tiled=True)


def unpack(sent):
    return sent.reshape(-1, sent.shape[2])


def local(tokens, routes, gate_codes, w_gate, w_up, w_down, cot):
    tok_rows, top = routes.shape
    width = tokens.shape[1]
    half = w_gate.shape[2]
    chips = lax.axis_size("dp") * lax.axis_size("x")
    pairs = tok_rows * top
    most = max(1, 2 * pairs // chips)
    slots = chips * most
    core = lax.axis_index("core")
    swap = [(0, 1), (1, 0)]
    f32 = jnp.float32

    wg_o, wu_o, wd_o = lax.ppermute((w_gate[0], w_up[0], w_down[0]), "core", swap)
    first = core == 0

    def halves(value):
        lo, hi = value[:, :half], value[:, half:]
        return jnp.where(first, lo, hi), jnp.where(first, hi, lo)

    wg = jnp.where(first, jnp.concatenate([w_gate[0], wg_o], 1), jnp.concatenate([wg_o, w_gate[0]], 1))
    wu = jnp.where(first, jnp.concatenate([w_up[0], wu_o], 1), jnp.concatenate([wu_o, w_up[0]], 1))
    wd = jnp.where(first, jnp.concatenate([w_down[0], wd_o], 0), jnp.concatenate([wd_o, w_down[0]], 0))

    expert_ids = routes.reshape(pairs)
    onehot = (expert_ids[:, None] == jnp.arange(chips, dtype=jnp.int32)[None, :]).astype(jnp.int32)
    before = jnp.cumsum(onehot, axis=0) - onehot
    position = jnp.sum(before * onehot, axis=1)
    slot = expert_ids * most + position
    gates = gate_codes.reshape(pairs).astype(f32) / 1024.0
    qpairs = (
        (gates.reshape(tok_rows, top, 1) * cot.astype(f32)[:, None, :])
        .astype(jnp.bfloat16)
        .reshape(pairs, width)
    )
    pick = slot.reshape(tok_rows, top).T[:, :, None] == jnp.arange(slots, dtype=jnp.int32)[None, None, :]
    pick = pick.astype(jnp.bfloat16)
    sel_x = (pick[0] + pick[1]).reshape(tok_rows, chips, most)
    sel_q = pick.transpose(2, 1, 0).reshape(chips, most, pairs)

    sel_x2 = sel_x.reshape(tok_rows, slots)
    xs = jnp.dot(sel_x2.T, tokens, preferred_element_type=f32).astype(jnp.bfloat16)
    xrows = to_chips(pack(xs, chips))
    qs = jnp.dot(sel_q.reshape(slots, pairs), qpairs, preferred_element_type=f32).astype(jnp.bfloat16)
    qs, xrows = lax.optimization_barrier((pack(qs, chips), xrows))
    xrows = unpack(xrows)
    qrows = to_chips(qs)

    act = jnp.dot(xrows, wg, preferred_element_type=f32)
    upv = jnp.dot(xrows, wu, preferred_element_type=f32)
    sig = jax.nn.sigmoid(act)
    silu = act * sig
    hidden = (silu * upv).astype(jnp.bfloat16)
    outv = jnp.dot(hidden, wd, preferred_element_type=f32).astype(jnp.bfloat16)
    qrows, outv = lax.optimization_barrier((qrows, pack(outv, chips)))
    qrows = unpack(qrows)
    o_back = to_chips(outv)

    dhid = jnp.dot(qrows, wd.T, preferred_element_type=f32)
    dact = (dhid * upv * sig * (1.0 + act * (1.0 - sig))).astype(jnp.bfloat16)
    dupv = (dhid * silu).astype(jnp.bfloat16)
    pgrad = (
        jnp.dot(dact, wg.T, preferred_element_type=f32)
        + jnp.dot(dupv, wu.T, preferred_element_type=f32)
    ).astype(jnp.bfloat16)
    hid_m, hid_o = halves(hidden)
    other_d = jnp.dot(hid_o.T, qrows, preferred_element_type=f32)
    pgrad, o_back, dact, dupv, hid_m, other_d = lax.optimization_barrier(
        (pack(pgrad, chips), o_back, dact, dupv, hid_m, other_d)
    )
    o_back = unpack(o_back)
    p_back = unpack(to_chips(pgrad))

    dact_m, dact_o = halves(dact)
    dupv_m, dupv_o = halves(dupv)
    other = (
        jnp.dot(xrows.T, dact_o, preferred_element_type=f32),
        jnp.dot(xrows.T, dupv_o, preferred_element_type=f32),
        other_d,
    )
    came = lax.ppermute(other, "core", swap)
    d_gate = (jnp.dot(xrows.T, dact_m, preferred_element_type=f32) + came[0]).astype(jnp.bfloat16)
    d_up = (jnp.dot(xrows.T, dupv_m, preferred_element_type=f32) + came[1]).astype(jnp.bfloat16)
    d_down = (jnp.dot(hid_m.T, qrows, preferred_element_type=f32) + came[2]).astype(jnp.bfloat16)

    o_k = jnp.einsum("kts,sw->ktw", pick, o_back, preferred_element_type=f32)
    mixed = (gates.reshape(tok_rows, top).T[:, :, None] * o_k).sum(0).astype(jnp.bfloat16)
    d_tokens = jnp.dot(sel_x2, p_back, preferred_element_type=f32).astype(jnp.bfloat16)
    return (mixed, d_tokens, d_gate[None], d_up[None], d_down[None])


def solution(mesh):
    n_data = mesh.shape["dp"]
    n_group = mesh.shape["expert"]
    fine = Mesh(mesh.devices.reshape(n_data, n_group // 2, 2), ("dp", "x", "core"))
    rows = P(("dp", "x", "core"), None)
    stack = P(("dp", "x", "core"), None, None)
    return jax.shard_map(
        local,
        mesh=fine,
        in_specs=(rows, rows, rows, stack, stack, stack, rows),
        out_specs=(rows, rows, stack, stack, stack),
        check_vma=False,
    )
```

```python
import jax
import jax.numpy as jnp
from jax import lax
from jax.sharding import Mesh
from jax.sharding import PartitionSpec as P

CHIPS = ("dp", "x")


def pack(rows, chips):
    return rows.reshape(chips, -1, rows.shape[1])


def to_chips(packed):
    return lax.all_to_all(packed, CHIPS, 0, 0, tiled=True)


def unpack(sent):
    return sent.reshape(-1, sent.shape[2])


def local(tokens, routes, gate_codes, w_gate, w_up, w_down, cot):
    tok_rows, top = routes.shape
    width = tokens.shape[1]
    half = w_gate.shape[2]
    chips = lax.axis_size("dp") * lax.axis_size("x")
    pairs = tok_rows * top
    most = max(1, 2 * pairs // chips)
    slots = chips * most
    core = lax.axis_index("core")
    swap = [(0, 1), (1, 0)]
    f32 = jnp.float32

    wg_o, wu_o, wd_o = lax.ppermute((w_gate[0], w_up[0], w_down[0]), "core", swap)
    first = core == 0
    wg = jnp.where(first, jnp.concatenate([w_gate[0], wg_o], 1), jnp.concatenate([wg_o, w_gate[0]], 1))
    wu = jnp.where(first, jnp.concatenate([w_up[0], wu_o], 1), jnp.concatenate([wu_o, w_up[0]], 1))
    wd = jnp.where(first, jnp.concatenate([w_down[0], wd_o], 0), jnp.concatenate([wd_o, w_down[0]], 0))

    expert_ids = routes.reshape(pairs)
    order = jnp.arange(pairs, dtype=jnp.int32)
    earlier = (expert_ids[:, None] == expert_ids[None, :]) & (order[None, :] < order[:, None])
    position = jnp.sum(earlier.astype(jnp.int32), axis=1)
    slot = expert_ids * most + position
    gates = gate_codes.reshape(pairs).astype(f32) / 1024.0
    qpairs = (
        (gates.reshape(tok_rows, top, 1) * cot.astype(f32)[:, None, :])
        .astype(jnp.bfloat16)
        .reshape(pairs, width)
    )
    pick = slot.reshape(tok_rows, top).T[:, :, None] == jnp.arange(slots, dtype=jnp.int32)[None, None, :]
    pick = pick.astype(jnp.bfloat16)
    sel_x = (pick[0] + pick[1]).reshape(tok_rows, chips, most)
    sel_q = pick.transpose(2, 1, 0).reshape(chips, most, pairs)

    sel_x2 = sel_x.reshape(tok_rows, slots)
    xs = jnp.dot(sel_x2.T, tokens, preferred_element_type=f32).astype(jnp.bfloat16)
    xrows = to_chips(pack(xs, chips))
    qs = jnp.dot(sel_q.reshape(slots, pairs), qpairs, preferred_element_type=f32).astype(jnp.bfloat16)
    qs, xrows = lax.optimization_barrier((pack(qs, chips), xrows))
    xrows = unpack(xrows)
    qrows = to_chips(qs)

    act = jnp.dot(xrows, wg, preferred_element_type=f32)
    upv = jnp.dot(xrows, wu, preferred_element_type=f32)
    sig = jax.nn.sigmoid(act)
    silu = act * sig
    hidden = (silu * upv).astype(jnp.bfloat16)
    outv = jnp.dot(hidden, wd, preferred_element_type=f32).astype(jnp.bfloat16)
    qrows, outv = lax.optimization_barrier((qrows, pack(outv, chips)))
    qrows = unpack(qrows)
    o_back = to_chips(outv)

    dhid = jnp.dot(qrows, wd.T, preferred_element_type=f32)
    dact = (dhid * upv * sig * (1.0 + act * (1.0 - sig))).astype(jnp.bfloat16)
    dupv = (dhid * silu).astype(jnp.bfloat16)
    pgrad = (
        jnp.dot(dact, wg.T, preferred_element_type=f32)
        + jnp.dot(dupv, wu.T, preferred_element_type=f32)
    ).astype(jnp.bfloat16)
    pgrad, o_back, dact, dupv, hidden = lax.optimization_barrier((pack(pgrad, chips), o_back, dact, dupv, hidden))
    o_back = unpack(o_back)
    p_back = unpack(to_chips(pgrad))

    grad_g = jnp.dot(xrows.T, dact, preferred_element_type=f32)
    grad_u = jnp.dot(xrows.T, dupv, preferred_element_type=f32)
    grad_d = jnp.dot(hidden.T, qrows, preferred_element_type=f32)
    g_lo, g_hi = grad_g[:, :half], grad_g[:, half:]
    u_lo, u_hi = grad_u[:, :half], grad_u[:, half:]
    d_lo, d_hi = grad_d[:half], grad_d[half:]
    mine = (jnp.where(first, g_lo, g_hi), jnp.where(first, u_lo, u_hi), jnp.where(first, d_lo, d_hi))
    other = (jnp.where(first, g_hi, g_lo), jnp.where(first, u_hi, u_lo), jnp.where(first, d_hi, d_lo))
    came = lax.ppermute(other, "core", swap)
    d_gate = (mine[0] + came[0]).astype(jnp.bfloat16)
    d_up = (mine[1] + came[1]).astype(jnp.bfloat16)
    d_down = (mine[2] + came[2]).astype(jnp.bfloat16)

    o_k = jnp.einsum("kts,sw->ktw", pick, o_back, preferred_element_type=f32)
    mixed = (gates.reshape(tok_rows, top).T[:, :, None] * o_k).sum(0).astype(jnp.bfloat16)
    d_tokens = jnp.dot(sel_x2, p_back, preferred_element_type=f32).astype(jnp.bfloat16)
    return (mixed, d_tokens, d_gate[None], d_up[None], d_down[None])


def solution(mesh):
    n_data = mesh.shape["dp"]
    n_group = mesh.shape["expert"]
    fine = Mesh(mesh.devices.reshape(n_data, n_group // 2, 2), ("dp", "x", "core"))
    rows = P(("dp", "x", "core"), None)
    stack = P(("dp", "x", "core"), None, None)
    return jax.shard_map(
        local,
        mesh=fine,
        in_specs=(rows, rows, rows, stack, stack, stack, rows),
        out_specs=(rows, rows, stack, stack, stack),
        check_vma=False,
    )
```

```python
import jax
import jax.numpy as jnp
from jax import lax
from jax.sharding import Mesh
from jax.sharding import PartitionSpec as P

CHIPS = ("dp", "x")


def pack(rows, chips):
    return rows.reshape(chips, -1, rows.shape[1])


def to_chips(packed):
    return lax.all_to_all(packed, CHIPS, 0, 0, tiled=True)


def unpack(sent):
    return sent.reshape(-1, sent.shape[2])


def local(tokens, routes, gate_codes, w_gate, w_up, w_down, cot):
    tok_rows, top = routes.shape
    width = tokens.shape[1]
    half = w_gate.shape[2]
    chips = lax.axis_size("dp") * lax.axis_size("x")
    pairs = tok_rows * top
    most = max(1, 2 * pairs // chips)
    slots = chips * most
    core = lax.axis_index("core")
    swap = [(0, 1), (1, 0)]
    f32 = jnp.float32

    wg_o, wu_o, wd_o = lax.ppermute((w_gate[0], w_up[0], w_down[0]), "core", swap)
    first = core == 0

    def halves(value):
        lo, hi = value[:, :half], value[:, half:]
        return jnp.where(first, lo, hi), jnp.where(first, hi, lo)

    wg = jnp.where(first, jnp.concatenate([w_gate[0], wg_o], 1), jnp.concatenate([wg_o, w_gate[0]], 1))
    wu = jnp.where(first, jnp.concatenate([w_up[0], wu_o], 1), jnp.concatenate([wu_o, w_up[0]], 1))
    wd = jnp.where(first, jnp.concatenate([w_down[0], wd_o], 0), jnp.concatenate([wd_o, w_down[0]], 0))

    expert_ids = routes.reshape(pairs)
    order = jnp.arange(pairs, dtype=jnp.int32)
    earlier = (expert_ids[:, None] == expert_ids[None, :]) & (order[None, :] < order[:, None])
    position = jnp.sum(earlier.astype(jnp.int32), axis=1)
    slot = expert_ids * most + position
    gates = gate_codes.reshape(pairs).astype(f32) / 1024.0
    qpairs = (
        (gates.reshape(tok_rows, top, 1) * cot.astype(f32)[:, None, :])
        .astype(jnp.bfloat16)
        .reshape(pairs, width)
    )
    pick = slot.reshape(tok_rows, top).T[:, :, None] == jnp.arange(slots, dtype=jnp.int32)[None, None, :]
    pick = pick.astype(jnp.bfloat16)
    sel_x = (pick[0] + pick[1]).reshape(tok_rows, chips, most)
    sel_q = pick.transpose(2, 1, 0).reshape(chips, most, pairs)

    sel_x2 = sel_x.reshape(tok_rows, slots)
    xs = jnp.dot(sel_x2.T, tokens, preferred_element_type=f32).astype(jnp.bfloat16)
    xrows = to_chips(pack(xs, chips))
    qs = jnp.dot(sel_q.reshape(slots, pairs), qpairs, preferred_element_type=f32).astype(jnp.bfloat16)
    qs, xrows = lax.optimization_barrier((pack(qs, chips), xrows))
    xrows = unpack(xrows)
    qrows = to_chips(qs)

    act = jnp.dot(xrows, wg, preferred_element_type=f32)
    upv = jnp.dot(xrows, wu, preferred_element_type=f32)
    sig = jax.nn.sigmoid(act)
    silu = act * sig
    hidden = (silu * upv).astype(jnp.bfloat16)
    outv = jnp.dot(hidden, wd, preferred_element_type=f32).astype(jnp.bfloat16)
    qrows, outv = lax.optimization_barrier((qrows, pack(outv, chips)))
    qrows = unpack(qrows)
    o_back = to_chips(outv)

    dhid = jnp.dot(qrows, wd.T, preferred_element_type=f32)
    dact = (dhid * upv * sig * (1.0 + act * (1.0 - sig))).astype(jnp.bfloat16)
    dupv = (dhid * silu).astype(jnp.bfloat16)
    pgrad = (
        jnp.dot(dact, wg.T, preferred_element_type=f32)
        + jnp.dot(dupv, wu.T, preferred_element_type=f32)
    ).astype(jnp.bfloat16)
    hid_m, hid_o = halves(hidden)
    other_d = jnp.dot(hid_o.T, qrows, preferred_element_type=f32)
    pgrad, o_back, dact, dupv, hid_m, other_d = lax.optimization_barrier(
        (pack(pgrad, chips), o_back, dact, dupv, hid_m, other_d)
    )
    o_back = unpack(o_back)
    p_back = unpack(to_chips(pgrad))

    dact_m, dact_o = halves(dact)
    dupv_m, dupv_o = halves(dupv)
    other = (
        jnp.dot(xrows.T, dact_o, preferred_element_type=f32),
        jnp.dot(xrows.T, dupv_o, preferred_element_type=f32),
        other_d,
    )
    came = lax.ppermute(other, "core", swap)
    d_gate = (jnp.dot(xrows.T, dact_m, preferred_element_type=f32) + came[0]).astype(jnp.bfloat16)
    d_up = (jnp.dot(xrows.T, dupv_m, preferred_element_type=f32) + came[1]).astype(jnp.bfloat16)
    d_down = (jnp.dot(hid_m.T, qrows, preferred_element_type=f32) + came[2]).astype(jnp.bfloat16)

    o_k = jnp.einsum("kts,sw->ktw", pick, o_back, preferred_element_type=f32)
    mixed = (gates.reshape(tok_rows, top).T[:, :, None] * o_k).sum(0).astype(jnp.bfloat16)
    d_tokens = jnp.dot(sel_x2, p_back, preferred_element_type=f32).astype(jnp.bfloat16)
    return (mixed, d_tokens, d_gate[None], d_up[None], d_down[None])


def solution(mesh):
    n_data = mesh.shape["dp"]
    n_group = mesh.shape["expert"]
    fine = Mesh(mesh.devices.reshape(n_data, n_group // 2, 2), ("dp", "x", "core"))
    rows = P(("dp", "x", "core"), None)
    stack = P(("dp", "x", "core"), None, None)
    return jax.shard_map(
        local,
        mesh=fine,
        in_specs=(rows, rows, rows, stack, stack, stack, rows),
        out_specs=(rows, rows, stack, stack, stack),
        check_vma=False,
    )
```
